256 devices in a mesh: tm: 32 (over x, z), scen: 8 (over y, core).
Axes of the slice: x: 4, y: 4, z: 8, core: 2. Of those that a mesh axis runs over, the one named last changes fastest.
Arguments:
- operators: float32 [32, 512, 512], P('tm'), may hold values from -1 to 1
- input_maps: bfloat16 [4, 512, 256], replicated, may hold values from -0.056152344 to 0.056152344
- segment: int32 [32], P('tm'), may hold values from 0 to 3
- load: bfloat16 [32, 512, 256], P('tm', 'scen'), may hold values from -6 to 6
- initial: float32 [512, 512], P('scen'), may hold values from -6 to 6
- observed: bfloat16 [32, 512, 2048], P('tm', 'scen'), may hold values from -6 to 6
Outputs:
- states: float32 [32, 512, 512], P('tm', 'scen')
- gram: float32 [512, 512], P('tm', 'scen')
- cross: float32 [512, 2048], P('tm', 'scen')
The draws below stay inside these ranges and needn't reach their ends.
All inputs are finite; a program needn't handle non-finite values.
Results may differ from the reference program's by a relative error of at most 0.0003.
Values sent between devices are 32-bit elements; how exact they have to be, the bound alone decides.
No kernel may reach another device: no remote copies, remote signals or barrier semaphores. Data moves between devices by JAX's collectives and lax.ppermute only.
A program may use at most 192 MiB of HBM per device.

```python
import jax
import jax.numpy as jnp
from jax import lax

R = 512
RACKS = 256
SENS = 2048
NSEG = 4
K = 1
TOTAL_STEPS = 32
SCEN = 512


def draw_operators(key, part):
    random_keys = jax.random.split(key, 7)
    share = 0.5
    fast_mode = jax.random.uniform(random_keys[0], (R,)) < share
    fast_rate = jax.random.uniform(random_keys[1], (R,), minval=1.0 / 50.0, maxval=1.0 / 30.0)
    slow_rate = jax.random.uniform(random_keys[2], (R,), minval=0.1 / TOTAL_STEPS, maxval=0.4 / TOTAL_STEPS)
    rates = jnp.where(fast_mode, fast_rate, slow_rate)
    block_factor = jax.random.uniform(random_keys[3], (TOTAL_STEPS // K,), minval=1.0, maxval=2.5)
    per_step = jnp.repeat(block_factor, K)
    damping_factor = jnp.exp(-rates[None, :] * per_step[:, None])
    time_points = jnp.arange(TOTAL_STEPS, dtype=jnp.int32)
    start_offset = jax.random.randint(random_keys[4], (), 0, max(TOTAL_STEPS // 2, 1))
    spike_start = (time_points == start_offset) | (time_points == start_offset + TOTAL_STEPS // 2)
    spike_magnitude = jax.random.uniform(random_keys[5], (TOTAL_STEPS,), minval=0.5, maxval=0.8)
    diagonal_entries = damping_factor * jnp.where(spike_start, spike_magnitude, 1.0)[:, None]
    noise = jax.random.normal(random_keys[6], (TOTAL_STEPS, R, R), jnp.float32) * (0.06 / R ** 0.5)
    coupling = noise - jnp.transpose(noise, (0, 2, 1))
    matrices = coupling + diagonal_entries[:, :, None] * jnp.eye(R, dtype=jnp.float32)[None, :, :]
    return matrices.astype(jnp.float32)


def with_ends(values, own_key, smallest, largest):
    shape = values.shape
    spot = [jax.random.randint(jax.random.fold_in(own_key, axis), (), 0, shape[axis]) for axis in range(len(shape))]
    values = values.at[tuple(spot)].set(smallest)
    longest = shape.index(max(shape))
    spot[longest] = (spot[longest] + 1) % shape[longest]
    return values.at[tuple(spot)].set(largest)


def shard_levels(rng, dims, cuts, least, high):
    gain, own = 1.0, jax.random.fold_in(rng, 6)
    for axis_at, parts in cuts:
        draws = jnp.exp(jax.random.uniform(jax.random.fold_in(own, axis_at), (parts,), jnp.float32, least / len(cuts), high / len(cuts)))
        gain = gain * jnp.repeat(draws, dims[axis_at] // parts).reshape([-1 if axis == axis_at else 1 for axis in range(len(dims))])
    return gain


def normal_values(own_key, extent, deviation, most, pieces=(), kind=jnp.bfloat16):
    drawn = deviation * jax.random.normal(own_key, extent, jnp.float32)
    if pieces:
        drawn = drawn * shard_levels(own_key, extent, pieces, -0.22, 0.18)
    return jnp.clip(drawn, -most, most).astype(kind)


def setup_inputs(seed: int = 0) -> dict:
    key_of = jax.random.split(jax.random.key(seed), 7)
    operators = draw_operators(jax.random.fold_in(key_of[6], 71), 0)
    input_maps = normal_values(key_of[1], (NSEG, R, RACKS), (0.15 / RACKS ** 0.5), 0.056152344)
    segment = with_ends(jax.random.randint(key_of[2], (TOTAL_STEPS,), 0, NSEG), jax.random.fold_in(key_of[2], 1), 0, NSEG - 1).astype(jnp.int32)
    load = normal_values(key_of[3], (TOTAL_STEPS, SCEN, RACKS), 1.0, 6.0, ((0, 32), (1, 8)))
    initial = normal_values(key_of[4], (SCEN, R), 1.0, 6.0, ((0, 8),), jnp.float32)
    observed = normal_values(key_of[5], (TOTAL_STEPS, SCEN, SENS), 1.0, 6.0, ((0, 32), (1, 8)))
    return dict(operators=operators, input_maps=input_maps, segment=segment, load=load, initial=initial, observed=observed)


def reference(operators, input_maps, segment, load, initial, observed):
    highest = lax.Precision.HIGHEST
    regimes = jnp.arange(NSEG, dtype=jnp.int32)
    onehot = (segment[:, None] == regimes[None, :]).astype(jnp.float32)
    normalize = 1.0 / (TOTAL_STEPS * SCEN)

    def advance(carry, inputs):
        current, gram_sum, cross_sum = carry
        matrix, choose, rack_power, reading = inputs
        chosen = jnp.einsum('g,grk->rk', choose, input_maps.astype(jnp.float32)).astype(jnp.bfloat16)
        heating = jnp.dot(rack_power, chosen.T, preferred_element_type=jnp.float32)
        updated = jnp.einsum('sq,rq->sr', current, matrix, precision=highest) + heating
        gram_sum = gram_sum + jnp.einsum('sr,sq->rq', updated, updated, precision=highest)
        cross_sum = cross_sum + jnp.einsum('sr,so->ro', updated, reading.astype(jnp.float32), precision=highest)
        return (updated, gram_sum, cross_sum), updated

    begin = (initial, jnp.zeros((R, R), jnp.float32), jnp.zeros((R, SENS), jnp.float32))
    (last_state, gram_sum, cross_sum), states = lax.scan(advance, begin, (operators, onehot, load, observed))
    return states, gram_sum * normalize, cross_sum * normalize
```

```python
import jax
import jax.numpy as jnp
from jax import lax
from jax.sharding import PartitionSpec as P


def shift_scan(matrix, vector, axis):
    highest = lax.Precision.HIGHEST
    count, index = (lax.axis_size(axis), lax.axis_index(axis))
    distance = 1
    while distance < count:
        pairs = [(j, j + distance) for j in range(count - distance)]
        last = 2 * distance >= count
        has = index >= distance
        got_vector = lax.ppermute(vector, axis, pairs)
        if not last:
            got_matrix = lax.ppermute(matrix, axis, pairs)
        newer = jnp.einsum("sq,rq->sr", got_vector, matrix, precision=highest) + vector
        vector = jnp.where(has, newer, vector)
        if not last:
            joined = jnp.dot(matrix, got_matrix, precision=highest)
            matrix = jnp.where(has, joined, matrix)
        distance *= 2
    return vector


def halving_scatter(block, axis):
    count, index = (lax.axis_size(axis), lax.axis_index(axis))
    bit = count // 2
    while bit >= 1:
        half = block.shape[0] // 2
        upper = (index // bit) % 2 == 1
        low, high = block[:half], block[half:]
        keep = jnp.where(upper, high, low)
        send = jnp.where(upper, low, high)
        pairs = [(j, j ^ bit) for j in range(count)]
        block = keep + lax.ppermute(send, axis, pairs)
        bit //= 2
    return block


def on_device(operators, input_maps, segment, load, initial, observed):
    highest = lax.Precision.HIGHEST
    step_count = operators.shape[0]
    modes = operators.shape[1]
    local_scen = initial.shape[0]
    time_shards = lax.axis_size("tm")
    scen_shards = lax.axis_size("scen")
    regimes = jnp.arange(input_maps.shape[0], dtype=jnp.int32)
    onehot = (segment[:, None] == regimes[None, :]).astype(jnp.bfloat16)
    weighted = jnp.einsum(
        "tg,grk->trk", onehot, input_maps, preferred_element_type=jnp.float32
    ).astype(jnp.bfloat16)
    forcing = jnp.einsum("tsk,trk->tsr", load, weighted, preferred_element_type=jnp.float32)
    first_shard = lax.axis_index("tm") == 0
    anchor = jnp.where(first_shard, initial, jnp.zeros_like(initial))

    def advance(current, inputs):
        matrix, heating = inputs
        updated = jnp.einsum("sq,rq->sr", current, matrix, precision=highest) + heating
        return (updated, updated)

    last_state, local_states = lax.scan(advance, anchor, (operators, forcing))
    identity_matrix = jnp.eye(modes, dtype=jnp.float32)

    def compose_step(product, matrix):
        newer = jnp.dot(matrix, product, precision=highest)
        return (newer, newer)

    composed, products = lax.scan(compose_step, identity_matrix, operators)
    composed = jnp.where(first_shard, jnp.zeros_like(composed), composed)
    leaving = shift_scan(composed, last_state, "tm")
    if step_count == 1:
        states = leaving[None]
    else:
        pairs = [(j, j + 1) for j in range(time_shards - 1)]
        entering = lax.ppermute(leaving, "tm", pairs)
        states = local_states + jnp.einsum("sq,trq->tsr", entering, products, precision=highest)
    normalize = 1.0 / (step_count * time_shards * local_scen * scen_shards)
    gram_term = jnp.einsum("tsr,tsq->rq", states, states, precision=highest) * normalize
    cross_term = (
        jnp.einsum("tsr,tso->ro", states, observed.astype(jnp.float32), precision=highest)
        * normalize
    )
    gram_cols = gram_term.shape[1] // scen_shards
    cross_cols = cross_term.shape[1] // scen_shards
    joined = jnp.concatenate(
        [
            gram_term.reshape(modes, scen_shards, gram_cols),
            cross_term.reshape(modes, scen_shards, cross_cols),
        ],
        axis=2,
    ).reshape(modes, scen_shards * (gram_cols + cross_cols))
    partial = lax.psum_scatter(joined, "scen", scatter_dimension=1, tiled=True)
    mine = halving_scatter(partial, "tm")
    return (states, mine[:, :gram_cols], mine[:, gram_cols:])


def solution(mesh):
    in_specs = (
        P("tm", None, None),
        P(),
        P("tm"),
        P("tm", "scen", None),
        P("scen", None),
        P("tm", "scen", None),
    )
    out_specs = (P("tm", "scen", None), P("tm", "scen"), P("tm", "scen"))
    return jax.shard_map(
        on_device, mesh=mesh, in_specs=in_specs, out_specs=out_specs, check_vma=False
    )
```

```python
import jax
import jax.numpy as jnp
from jax import lax
from jax.sharding import PartitionSpec as P


def shift_scan(matrix, vector, axis, pair_axis):
    highest = lax.Precision.HIGHEST
    count, index = (lax.axis_size(axis), lax.axis_index(axis))
    pair_count = lax.axis_size(pair_axis)
    side = lax.axis_index(pair_axis) % 2
    width = matrix.shape[1] // 2
    swap = [(j, j ^ 1) for j in range(pair_count)]
    distance = 1
    while distance < count:
        pairs = [(j, j + distance) for j in range(count - distance)]
        last = 2 * distance >= count
        has = index >= distance
        got_vector = lax.ppermute(vector, axis, pairs)
        if not last:
            mine = lax.dynamic_slice_in_dim(matrix, side * width, width, axis=1)
            got_half = lax.ppermute(mine, axis, pairs)
        newer = jnp.einsum("sq,rq->sr", got_vector, matrix, precision=highest) + vector
        vector = jnp.where(has, newer, vector)
        if not last:
            own = jnp.dot(matrix, got_half, precision=highest)
            other = lax.ppermute(own, pair_axis, swap)
            joined = jnp.where(
                side == 0,
                jnp.concatenate([own, other], axis=1),
                jnp.concatenate([other, own], axis=1),
            )
            matrix = jnp.where(has, joined, matrix)
        distance *= 2
    return vector


def halving_scatter(block, axis):
    count, index = (lax.axis_size(axis), lax.axis_index(axis))
    bit = count // 2
    while bit >= 1:
        half = block.shape[0] // 2
        upper = (index // bit) % 2 == 1
        low, high = block[:half], block[half:]
        keep = jnp.where(upper, high, low)
        send = jnp.where(upper, low, high)
        pairs = [(j, j ^ bit) for j in range(count)]
        block = keep + lax.ppermute(send, axis, pairs)
        bit //= 2
    return block


def on_device(operators, input_maps, segment, load, initial, observed):
    highest = lax.Precision.HIGHEST
    step_count = operators.shape[0]
    modes = operators.shape[1]
    local_scen = initial.shape[0]
    time_shards = lax.axis_size("tm")
    scen_shards = lax.axis_size("scen")
    regimes = jnp.arange(input_maps.shape[0], dtype=jnp.int32)
    onehot = (segment[:, None] == regimes[None, :]).astype(jnp.bfloat16)
    weighted = jnp.einsum(
        "tg,grk->trk", onehot, input_maps, preferred_element_type=jnp.float32
    ).astype(jnp.bfloat16)
    forcing = jnp.einsum("tsk,trk->tsr", load, weighted, preferred_element_type=jnp.float32)
    first_shard = lax.axis_index("tm") == 0
    anchor = jnp.where(first_shard, initial, jnp.zeros_like(initial))

    def advance(current, inputs):
        matrix, heating = inputs
        updated = jnp.einsum("sq,rq->sr", current, matrix, precision=highest) + heating
        return (updated, updated)

    last_state, local_states = lax.scan(advance, anchor, (operators, forcing))
    identity_matrix = jnp.eye(modes, dtype=jnp.float32)

    def compose_step(product, matrix):
        newer = jnp.dot(matrix, product, precision=highest)
        return (newer, newer)

    composed, products = lax.scan(compose_step, identity_matrix, operators)
    composed = jnp.where(first_shard, jnp.zeros_like(composed), composed)
    leaving = shift_scan(composed, last_state, "tm", "scen")
    if step_count == 1:
        states = leaving[None]
    else:
        pairs = [(j, j + 1) for j in range(time_shards - 1)]
        entering = lax.ppermute(leaving, "tm", pairs)
        states = local_states + jnp.einsum("sq,trq->tsr", entering, products, precision=highest)
    normalize = 1.0 / (step_count * time_shards * local_scen * scen_shards)
    gram_term = jnp.einsum("tsr,tsq->rq", states, states, precision=highest) * normalize
    cross_term = (
        jnp.einsum("tsr,tso->ro", states, observed.astype(jnp.float32), precision=highest)
        * normalize
    )
    gram_cols = gram_term.shape[1] // scen_shards
    cross_cols = cross_term.shape[1] // scen_shards
    joined = jnp.concatenate(
        [
            gram_term.reshape(modes, scen_shards, gram_cols),
            cross_term.reshape(modes, scen_shards, cross_cols),
        ],
        axis=2,
    ).reshape(modes, scen_shards * (gram_cols + cross_cols))
    partial = lax.psum_scatter(joined, "scen", scatter_dimension=1, tiled=True)
    mine = halving_scatter(partial, "tm")
    return (states, mine[:, :gram_cols], mine[:, gram_cols:])


def solution(mesh):
    in_specs = (
        P("tm", None, None),
        P(),
        P("tm"),
        P("tm", "scen", None),
        P("scen", None),
        P("tm", "scen", None),
    )
    out_specs = (P("tm", "scen", None), P("tm", "scen"), P("tm", "scen"))
    return jax.shard_map(
        on_device, mesh=mesh, in_specs=in_specs, out_specs=out_specs, check_vma=False
    )
```

```python
import jax
import jax.numpy as jnp
from jax import lax
from jax.sharding import PartitionSpec as P


def shift_scan(matrix, vector, axis, pair_axis):
    highest = lax.Precision.HIGHEST
    count, index = (lax.axis_size(axis), lax.axis_index(axis))
    pair_count = lax.axis_size(pair_axis)
    side = lax.axis_index(pair_axis) % 2
    width = matrix.shape[1] // 2
    swap = [(j, j ^ 1) for j in range(pair_count)]
    distance = 1
    while distance < count:
        pairs = [(j, j + distance) for j in range(count - distance)]
        last = 2 * distance >= count
        has = index >= distance
        got_vector = lax.ppermute(vector, axis, pairs)
        if not last:
            mine = lax.dynamic_slice_in_dim(matrix, side * width, width, axis=1)
            got_half = lax.ppermute(mine, axis, pairs)
        newer = jnp.einsum("sq,rq->sr", got_vector, matrix, precision=highest) + vector
        vector = jnp.where(has, newer, vector)
        if not last:
            own = jnp.dot(matrix, got_half, precision=highest)
            other = lax.ppermute(own, pair_axis, swap)
            joined = jnp.where(
                side == 0,
                jnp.concatenate([own, other], axis=1),
                jnp.concatenate([other, own], axis=1),
            )
            matrix = jnp.where(has, joined, matrix)
        distance = distance * 2
    return vector


def halving_scatter(block, axis):
    count, index = (lax.axis_size(axis), lax.axis_index(axis))
    bit = count // 2
    while bit >= 1:
        half = block.shape[0] // 2
        upper = (index // bit) % 2 == 1
        low, high = block[:half], block[half:]
        keep = jnp.where(upper, high, low)
        send = jnp.where(upper, low, high)
        pairs = [(j, j ^ bit) for j in range(count)]
        block = keep + lax.ppermute(send, axis, pairs)
        bit //= 2
    return block


def on_device_body(operators, input_maps, segment, load, initial, observed):
    highest = lax.Precision.HIGHEST
    step_count = operators.shape[0]
    modes = operators.shape[1]
    local_scen = initial.shape[0]
    time_shards = lax.axis_size("tm")
    scen_shards = lax.axis_size("scen")
    regimes = jnp.arange(input_maps.shape[0], dtype=jnp.int32)
    onehot = (segment[:, None] == regimes[None, :]).astype(jnp.bfloat16)
    weighted = jnp.einsum(
        "tg,grk->trk", onehot, input_maps, preferred_element_type=jnp.float32
    ).astype(jnp.bfloat16)
    forcing = jnp.einsum("tsk,trk->tsr", load, weighted, preferred_element_type=jnp.float32)
    first_shard = lax.axis_index("tm") == 0
    anchor = jnp.where(first_shard, initial, jnp.zeros_like(initial))

    def advance(current, inputs):
        matrix, heating = inputs
        updated = jnp.einsum("sq,rq->sr", current, matrix, precision=highest) + heating
        return (updated, updated)

    last_state, local_states = lax.scan(advance, anchor, (operators, forcing))
    identity_matrix = jnp.eye(modes, dtype=jnp.float32)

    def compose_step(product, matrix):
        newer = jnp.dot(matrix, product, precision=highest)
        return (newer, newer)

    composed, products = lax.scan(compose_step, identity_matrix, operators)
    composed = jnp.where(first_shard, jnp.zeros_like(composed), composed)
    leaving = shift_scan(composed, last_state, "tm", "scen")
    if step_count == 1:
        states = leaving[None]
    else:
        pairs = [(j, j + 1) for j in range(time_shards - 1)]
        entering = lax.ppermute(leaving, "tm", pairs)
        states = local_states + jnp.einsum("sq,trq->tsr", entering, products, precision=highest)
    normalize = 1.0 / (step_count * time_shards * local_scen * scen_shards)
    sensors = observed.shape[2]
    cross_cols = sensors // scen_shards
    gram_cols = modes // scen_shards
    readings = observed.astype(jnp.float32).reshape(step_count * local_scen, scen_shards, cross_cols)
    readings = lax.all_to_all(readings, "scen", 1, 0, tiled=True)
    readings = readings.reshape(scen_shards, step_count, local_scen, cross_cols)
    readings = readings.transpose(1, 0, 2, 3).reshape(step_count, scen_shards * local_scen, cross_cols)
    every = lax.all_gather(states, "scen", axis=1, tiled=True)
    column = lax.axis_index("scen") * gram_cols
    right = jnp.concatenate(
        [lax.dynamic_slice_in_dim(every, column, gram_cols, axis=2), readings], axis=2
    )
    joined = jnp.einsum("tsr,tso->ro", every, right, precision=highest) * normalize
    mine = halving_scatter(joined, "tm")
    return (states, mine[:, :gram_cols], mine[:, gram_cols:])


def solution(mesh):
    in_specs = (
        P("tm", None, None),
        P(),
        P("tm"),
        P("tm", "scen", None),
        P("scen", None),
        P("tm", "scen", None),
    )
    out_specs = (P("tm", "scen", None), P("tm", "scen"), P("tm", "scen"))
    return jax.shard_map(
        on_device_body, mesh=mesh, in_specs=in_specs, out_specs=out_specs, check_vma=False
    )
```

```python
import jax
import jax.numpy as jnp
from jax import lax
from jax.sharding import PartitionSpec as P


def shift_scan(matrix, vector, axis, pair_axis):
    highest = lax.Precision.HIGHEST
    count, index = (lax.axis_size(axis), lax.axis_index(axis))
    pair_count = lax.axis_size(pair_axis)
    side = lax.axis_index(pair_axis) % 2
    width = matrix.shape[1] // 2
    swap = [(j, j ^ 1) for j in range(pair_count)]
    distance = 1
    while distance < count:
        pairs = [(j, j + distance) for j in range(count - distance)]
        last = 2 * distance >= count
        has = index >= distance
        got_vector = lax.ppermute(vector, axis, pairs)
        if not last:
            mine = lax.dynamic_slice_in_dim(matrix, side * width, width, axis=1)
            got_half = lax.ppermute(mine, axis, pairs)
        newer = jnp.einsum("sq,rq->sr", got_vector, matrix, precision=highest) + vector
        vector = jnp.where(has, newer, vector)
        if not last:
            own = jnp.dot(matrix, got_half, precision=highest)
            other = lax.ppermute(own, pair_axis, swap)
            joined = jnp.where(
                side == 0,
                jnp.concatenate([own, other], axis=1),
                jnp.concatenate([other, own], axis=1),
            )
            matrix = jnp.where(has, joined, matrix)
        distance = distance * 2
    return vector


def shift_scatter(block, axis, groups):
    count, index = (lax.axis_size(axis), lax.axis_index(axis))
    stride = count
    for size in groups:
        stride //= size
        place = (index // stride) % size
        chunk = block.shape[0] // size
        total = lax.dynamic_slice_in_dim(block, place * chunk, chunk, axis=0)
        for shift in range(1, size):
            pairs = []
            for j in range(count):
                at = (j // stride) % size
                pairs.append((j, j + (((at + shift) % size) - at) * stride))
            target = (place + shift) % size
            send = lax.dynamic_slice_in_dim(block, target * chunk, chunk, axis=0)
            total = total + lax.ppermute(send, axis, pairs)
        block = total
    return block


def shift_gather(piece, axis, dimension):
    count, index = (lax.axis_size(axis), lax.axis_index(axis))
    parts = [piece]
    for shift in range(1, count):
        pairs = [(j, (j + shift) % count) for j in range(count)]
        parts.append(lax.ppermute(piece, axis, pairs))
    stacked = jnp.stack(parts, axis=0)
    order = (index - jnp.arange(count)) % count
    rolled = jnp.take(stacked, jnp.argsort(order), axis=0)
    moved = jnp.moveaxis(rolled, 0, dimension)
    shape = list(piece.shape)
    shape[dimension] *= count
    return moved.reshape(shape)


def on_device_body(tm_groups, operators, input_maps, segment, load, initial, observed):
    highest = lax.Precision.HIGHEST
    step_count = operators.shape[0]
    modes = operators.shape[1]
    local_scen = initial.shape[0]
    time_shards = lax.axis_size("tm")
    scen_shards = lax.axis_size("scen")
    regimes = jnp.arange(input_maps.shape[0], dtype=jnp.int32)
    onehot = (segment[:, None] == regimes[None, :]).astype(jnp.bfloat16)
    weighted = jnp.einsum(
        "tg,grk->trk", onehot, input_maps, preferred_element_type=jnp.float32
    ).astype(jnp.bfloat16)
    forcing = jnp.einsum("tsk,trk->tsr", load, weighted, preferred_element_type=jnp.float32)
    first_shard = lax.axis_index("tm") == 0
    anchor = jnp.where(first_shard, initial, jnp.zeros_like(initial))

    def advance(current, inputs):
        matrix, heating = inputs
        updated = jnp.einsum("sq,rq->sr", current, matrix, precision=highest) + heating
        return (updated, updated)

    last_state, local_states = lax.scan(advance, anchor, (operators, forcing))
    identity_matrix = jnp.eye(modes, dtype=jnp.float32)

    def compose_step(product, matrix):
        newer = jnp.dot(matrix, product, precision=highest)
        return (newer, newer)

    composed, products = lax.scan(compose_step, identity_matrix, operators)
    composed = jnp.where(first_shard, jnp.zeros_like(composed), composed)
    leaving = shift_scan(composed, last_state, "tm", "scen")
    if step_count == 1:
        states = leaving[None]
    else:
        pairs = [(j, j + 1) for j in range(time_shards - 1)]
        entering = lax.ppermute(leaving, "tm", pairs)
        states = local_states + jnp.einsum("sq,trq->tsr", entering, products, precision=highest)
    normalize = 1.0 / (step_count * time_shards * local_scen * scen_shards)
    sensors = observed.shape[2]
    cross_cols = sensors // scen_shards
    gram_cols = modes // scen_shards
    readings = observed.astype(jnp.float32).reshape(step_count * local_scen, scen_shards, cross_cols)
    readings = lax.all_to_all(readings, "scen", 1, 0, tiled=True)
    readings = readings.reshape(scen_shards, step_count, local_scen, cross_cols)
    readings = readings.transpose(1, 0, 2, 3).reshape(step_count, scen_shards * local_scen, cross_cols)
    every = shift_gather(states, "scen", 1)
    column = lax.axis_index("scen") * gram_cols
    right = jnp.concatenate(
        [lax.dynamic_slice_in_dim(every, column, gram_cols, axis=2), readings], axis=2
    )
    joined = jnp.einsum("tsr,tso->ro", every, right, precision=highest) * normalize
    mine = shift_scatter(joined, "tm", tm_groups)
    return (states, mine[:, :gram_cols], mine[:, gram_cols:])


def solution(mesh):
    in_specs = (
        P("tm", None, None),
        P(),
        P("tm"),
        P("tm", "scen", None),
        P("scen", None),
        P("tm", "scen", None),
    )
    out_specs = (P("tm", "scen", None), P("tm", "scen"), P("tm", "scen"))
    count = dict(zip(mesh.axis_names, mesh.devices.shape))["tm"]
    tm_groups = (count // 8, 8) if count % 8 == 0 and count > 8 else (count,)

    def on_device(*args):
        return on_device_body(tm_groups, *args)

    return jax.shard_map(
        on_device, mesh=mesh, in_specs=in_specs, out_specs=out_specs, check_vma=False
    )
```

```python
import jax
import jax.numpy as jnp
from jax import lax
from jax.sharding import PartitionSpec as P


def shift_scan(matrix, vector, axis, pair_axis):
    highest = lax.Precision.HIGHEST
    count, index = (lax.axis_size(axis), lax.axis_index(axis))
    pair_count = lax.axis_size(pair_axis)
    side = lax.axis_index(pair_axis) % 2
    width = matrix.shape[1] // 2
    swap = [(j, j ^ 1) for j in range(pair_count)]
    mine = lax.dynamic_slice_in_dim(matrix, side * width, width, axis=1)
    distance = 1
    while distance < count:
        pairs = [(j, j + distance) for j in range(count - distance)]
        last = 2 * distance >= count
        has = index >= distance
        got_vector = lax.ppermute(vector, axis, pairs)
        if not last:
            got_half = lax.ppermute(mine, axis, pairs)
        newer = jnp.einsum("sq,rq->sr", got_vector, matrix, precision=highest) + vector
        vector = jnp.where(has, newer, vector)
        if not last:
            own = jnp.dot(matrix, got_half, precision=highest)
            other = lax.ppermute(own, pair_axis, swap)
            joined = jnp.where(
                side == 0,
                jnp.concatenate([own, other], axis=1),
                jnp.concatenate([other, own], axis=1),
            )
            matrix = jnp.where(has, joined, matrix)
            mine = jnp.where(has, own, mine)
        distance = distance * 2
    return vector


def on_device_body(operators, input_maps, segment, load, initial, observed):
    highest = lax.Precision.HIGHEST
    step_count = operators.shape[0]
    modes = operators.shape[1]
    local_scen = initial.shape[0]
    time_shards = lax.axis_size("tm")
    scen_shards = lax.axis_size("scen")
    regimes = jnp.arange(input_maps.shape[0], dtype=jnp.int32)
    onehot = (segment[:, None] == regimes[None, :]).astype(jnp.bfloat16)
    weighted = jnp.einsum(
        "tg,grk->trk", onehot, input_maps, preferred_element_type=jnp.float32
    ).astype(jnp.bfloat16)
    forcing = jnp.einsum("tsk,trk->tsr", load, weighted, preferred_element_type=jnp.float32)
    first_shard = lax.axis_index("tm") == 0
    anchor = jnp.where(first_shard, initial, jnp.zeros_like(initial))

    def advance(current, inputs):
        matrix, heating = inputs
        updated = jnp.einsum("sq,rq->sr", current, matrix, precision=highest) + heating
        return (updated, updated)

    last_state, local_states = lax.scan(advance, anchor, (operators, forcing))
    identity_matrix = jnp.eye(modes, dtype=jnp.float32)

    def compose_step(product, matrix):
        newer = jnp.dot(matrix, product, precision=highest)
        return (newer, newer)

    composed, products = lax.scan(compose_step, identity_matrix, operators)
    composed = jnp.where(first_shard, jnp.zeros_like(composed), composed)
    leaving = shift_scan(composed, last_state, "tm", "scen")
    if step_count == 1:
        states = leaving[None]
    else:
        pairs = [(j, j + 1) for j in range(time_shards - 1)]
        entering = lax.ppermute(leaving, "tm", pairs)
        states = local_states + jnp.einsum("sq,trq->tsr", entering, products, precision=highest)
    normalize = 1.0 / (step_count * time_shards * local_scen * scen_shards)
    sensors = observed.shape[2]
    cross_cols = sensors // scen_shards
    gram_cols = modes // scen_shards
    readings = observed.astype(jnp.float32).reshape(step_count * local_scen, scen_shards, cross_cols)
    readings = lax.all_to_all(readings, "scen", 1, 0, tiled=True)
    readings = readings.reshape(scen_shards, step_count, local_scen, cross_cols)
    readings = readings.transpose(1, 0, 2, 3).reshape(step_count, scen_shards * local_scen, cross_cols)
    every = lax.all_to_all(
        jnp.broadcast_to(states[None], (scen_shards,) + states.shape), "scen", 0, 0, tiled=True
    )
    every = every.reshape(scen_shards, step_count, local_scen, modes).transpose(1, 0, 2, 3)
    every = every.reshape(step_count, scen_shards * local_scen, modes)
    column = lax.axis_index("scen") * gram_cols
    right = jnp.concatenate(
        [lax.dynamic_slice_in_dim(every, column, gram_cols, axis=2), readings], axis=2
    )
    joined = jnp.einsum("tsr,tso->ro", every, right, precision=highest) * normalize
    pieces = joined.reshape(time_shards, modes // time_shards, joined.shape[1])
    mine = lax.all_to_all(pieces, "tm", 0, 0, tiled=True).sum(axis=0)
    return (states, mine[:, :gram_cols], mine[:, gram_cols:])


def solution(mesh):
    in_specs = (
        P("tm", None, None),
        P(),
        P("tm"),
        P("tm", "scen", None),
        P("scen", None),
        P("tm", "scen", None),
    )
    out_specs = (P("tm", "scen", None), P("tm", "scen"), P("tm", "scen"))

    return jax.shard_map(
        on_device_body, mesh=mesh, in_specs=in_specs, out_specs=out_specs, check_vma=False
    )
```

```python
import jax
import jax.numpy as jnp
from jax import lax
from jax.sharding import PartitionSpec as P


def shift_scan(matrix, vector, axis, pair_axis):
    highest = lax.Precision.HIGHEST
    count, index = (lax.axis_size(axis), lax.axis_index(axis))
    pair_count = lax.axis_size(pair_axis)
    side = lax.axis_index(pair_axis) % 2
    width = matrix.shape[1] // 2
    swap = [(j, j ^ 1) for j in range(pair_count)]
    mine = lax.dynamic_slice_in_dim(matrix, side * width, width, axis=1)
    distance = 1
    while distance < count:
        pairs = [(j, j + distance) for j in range(count - distance)]
        last = 2 * distance >= count
        has = index >= distance
        if last:
            got_vector = lax.ppermute(vector, axis, pairs)
        else:
            packed = jnp.concatenate([vector.reshape(-1, width), mine], axis=0)
            got = lax.ppermute(packed, axis, pairs)
            got_vector = got[: vector.size // width].reshape(vector.shape)
            got_half = got[vector.size // width :]
        newer = jnp.einsum("sq,rq->sr", got_vector, matrix, precision=highest) + vector
        vector = jnp.where(has, newer, vector)
        if not last:
            own = jnp.dot(matrix, got_half, precision=highest)
            other = lax.ppermute(own, pair_axis, swap)
            joined = jnp.where(
                side == 0,
                jnp.concatenate([own, other], axis=1),
                jnp.concatenate([other, own], axis=1),
            )
            matrix = jnp.where(has, joined, matrix)
            mine = jnp.where(has, own, mine)
        distance = distance * 2
    return vector


def on_device_body(operators, input_maps, segment, load, initial, observed):
    highest = lax.Precision.HIGHEST
    step_count = operators.shape[0]
    modes = operators.shape[1]
    local_scen = initial.shape[0]
    time_shards = lax.axis_size("tm")
    scen_shards = lax.axis_size("scen")
    regimes = jnp.arange(input_maps.shape[0], dtype=jnp.int32)
    onehot = (segment[:, None] == regimes[None, :]).astype(jnp.bfloat16)
    weighted = jnp.einsum(
        "tg,grk->trk", onehot, input_maps, preferred_element_type=jnp.float32
    ).astype(jnp.bfloat16)
    forcing = jnp.einsum("tsk,trk->tsr", load, weighted, preferred_element_type=jnp.float32)
    first_shard = lax.axis_index("tm") == 0
    anchor = jnp.where(first_shard, initial, jnp.zeros_like(initial))

    def advance(current, inputs):
        matrix, heating = inputs
        updated = jnp.einsum("sq,rq->sr", current, matrix, precision=highest) + heating
        return (updated, updated)

    last_state, local_states = lax.scan(advance, anchor, (operators, forcing))
    identity_matrix = jnp.eye(modes, dtype=jnp.float32)

    def compose_step(product, matrix):
        newer = jnp.dot(matrix, product, precision=highest)
        return (newer, newer)

    composed, products = lax.scan(compose_step, identity_matrix, operators)
    composed = jnp.where(first_shard, jnp.zeros_like(composed), composed)
    leaving = shift_scan(composed, last_state, "tm", "scen")
    if step_count == 1:
        states = leaving[None]
    else:
        pairs = [(j, j + 1) for j in range(time_shards - 1)]
        entering = lax.ppermute(leaving, "tm", pairs)
        states = local_states + jnp.einsum("sq,trq->tsr", entering, products, precision=highest)
    normalize = 1.0 / (step_count * time_shards * local_scen * scen_shards)
    sensors = observed.shape[2]
    cross_cols = sensors // scen_shards
    gram_cols = modes // scen_shards
    readings = observed.astype(jnp.float32).reshape(step_count * local_scen, scen_shards, cross_cols)
    readings = lax.all_to_all(readings, "scen", 1, 0, tiled=True)
    readings = readings.reshape(scen_shards, step_count, local_scen, cross_cols)
    readings = readings.transpose(1, 0, 2, 3).reshape(step_count, scen_shards * local_scen, cross_cols)
    every = lax.all_to_all(
        jnp.broadcast_to(states[None], (scen_shards,) + states.shape), "scen", 0, 0, tiled=True
    )
    every = every.reshape(scen_shards, step_count, local_scen, modes).transpose(1, 0, 2, 3)
    every = every.reshape(step_count, scen_shards * local_scen, modes)
    column = lax.axis_index("scen") * gram_cols
    right = jnp.concatenate(
        [lax.dynamic_slice_in_dim(every, column, gram_cols, axis=2), readings], axis=2
    )
    joined = jnp.einsum("tsr,tso->ro", every, right, precision=highest) * normalize
    pieces = joined.reshape(time_shards, modes // time_shards, joined.shape[1])
    mine = lax.all_to_all(pieces, "tm", 0, 0, tiled=True).sum(axis=0)
    return (states, mine[:, :gram_cols], mine[:, gram_cols:])


def solution(mesh):
    in_specs = (
        P("tm", None, None),
        P(),
        P("tm"),
        P("tm", "scen", None),
        P("scen", None),
        P("tm", "scen", None),
    )
    out_specs = (P("tm", "scen", None), P("tm", "scen"), P("tm", "scen"))

    return jax.shard_map(
        on_device_body, mesh=mesh, in_specs=in_specs, out_specs=out_specs, check_vma=False
    )
```

```python
import jax
import jax.numpy as jnp
from jax import lax
from jax.sharding import PartitionSpec as P


def shift_scan(matrix, vector, axis, pair_axis):
    highest = lax.Precision.HIGHEST
    count, index = (lax.axis_size(axis), lax.axis_index(axis))
    pair_count = lax.axis_size(pair_axis)
    side = lax.axis_index(pair_axis) % 2
    width = matrix.shape[1] // 2
    swap = [(j, j ^ 1) for j in range(pair_count)]
    mine = lax.dynamic_slice_in_dim(matrix, side * width, width, axis=1)
    distance = 1
    while distance < count:
        pairs = [(j, j + distance) for j in range(count - distance)]
        last = 2 * distance >= count
        has = index >= distance
        got_vector = lax.ppermute(vector, axis, pairs)
        if not last:
            got_half = lax.ppermute(mine, axis, pairs)
        newer = jnp.einsum("sq,rq->sr", got_vector, matrix, precision=highest) + vector
        vector = jnp.where(has, newer, vector)
        if not last:
            own = jnp.dot(matrix, got_half, precision=highest)
            other = lax.ppermute(own, pair_axis, swap)
            joined = jnp.where(
                side == 0,
                jnp.concatenate([own, other], axis=1),
                jnp.concatenate([other, own], axis=1),
            )
            matrix = jnp.where(has, joined, matrix)
            mine = jnp.where(has, own, mine)
        distance = distance * 2
    return vector


def on_device_body(tm_groups, operators, input_maps, segment, load, initial, observed):
    highest = lax.Precision.HIGHEST
    step_count = operators.shape[0]
    modes = operators.shape[1]
    local_scen = initial.shape[0]
    time_shards = lax.axis_size("tm")
    scen_shards = lax.axis_size("scen")
    regimes = jnp.arange(input_maps.shape[0], dtype=jnp.int32)
    onehot = (segment[:, None] == regimes[None, :]).astype(jnp.bfloat16)
    weighted = jnp.einsum(
        "tg,grk->trk", onehot, input_maps, preferred_element_type=jnp.float32
    ).astype(jnp.bfloat16)
    forcing = jnp.einsum("tsk,trk->tsr", load, weighted, preferred_element_type=jnp.float32)
    first_shard = lax.axis_index("tm") == 0
    anchor = jnp.where(first_shard, initial, jnp.zeros_like(initial))

    def advance(current, inputs):
        matrix, heating = inputs
        updated = jnp.einsum("sq,rq->sr", current, matrix, precision=highest) + heating
        return (updated, updated)

    last_state, local_states = lax.scan(advance, anchor, (operators, forcing))
    identity_matrix = jnp.eye(modes, dtype=jnp.float32)

    def compose_step(product, matrix):
        newer = jnp.dot(matrix, product, precision=highest)
        return (newer, newer)

    composed, products = lax.scan(compose_step, identity_matrix, operators)
    composed = jnp.where(first_shard, jnp.zeros_like(composed), composed)
    leaving = shift_scan(composed, last_state, "tm", "scen")
    if step_count == 1:
        states = leaving[None]
    else:
        pairs = [(j, j + 1) for j in range(time_shards - 1)]
        entering = lax.ppermute(leaving, "tm", pairs)
        states = local_states + jnp.einsum("sq,trq->tsr", entering, products, precision=highest)
    normalize = 1.0 / (step_count * time_shards * local_scen * scen_shards)
    sensors = observed.shape[2]
    cross_cols = sensors // scen_shards
    gram_cols = modes // scen_shards
    readings = observed.astype(jnp.float32).reshape(step_count * local_scen, scen_shards, cross_cols)
    readings = lax.all_to_all(readings, "scen", 1, 0, tiled=True)
    readings = readings.reshape(scen_shards, step_count, local_scen, cross_cols)
    readings = readings.transpose(1, 0, 2, 3).reshape(step_count, scen_shards * local_scen, cross_cols)
    every = lax.all_to_all(
        jnp.broadcast_to(states[None], (scen_shards,) + states.shape), "scen", 0, 0, tiled=True
    )
    every = every.reshape(scen_shards, step_count, local_scen, modes).transpose(1, 0, 2, 3)
    every = every.reshape(step_count, scen_shards * local_scen, modes)
    column = lax.axis_index("scen") * gram_cols
    right = jnp.concatenate(
        [lax.dynamic_slice_in_dim(every, column, gram_cols, axis=2), readings], axis=2
    )
    joined = jnp.einsum("tsr,tso->ro", every, right, precision=highest) * normalize
    mine = joined
    stride = time_shards
    for size in tm_groups:
        stride //= size
        groups = [
            [base + k * stride for k in range(size)]
            for base in range(time_shards)
            if (base // stride) % size == 0
        ]
        pieces = mine.reshape(size, mine.shape[0] // size, mine.shape[1])
        mine = lax.all_to_all(pieces, "tm", 0, 0, tiled=True, axis_index_groups=groups).sum(axis=0)
    return (states, mine[:, :gram_cols], mine[:, gram_cols:])


def solution(mesh):
    in_specs = (
        P("tm", None, None),
        P(),
        P("tm"),
        P("tm", "scen", None),
        P("scen", None),
        P("tm", "scen", None),
    )
    out_specs = (P("tm", "scen", None), P("tm", "scen"), P("tm", "scen"))
    count = dict(zip(mesh.axis_names, mesh.devices.shape))["tm"]
    tm_groups = (count // 8, 8) if count % 8 == 0 and count > 8 else (count,)

    def on_device(*args):
        return on_device_body(tm_groups, *args)

    return jax.shard_map(
        on_device, mesh=mesh, in_specs=in_specs, out_specs=out_specs, check_vma=False
    )
```

```python
import jax
import jax.numpy as jnp
from jax import lax
from jax.sharding import PartitionSpec as P


def shift_scan(matrix, vector, axis, pair_axis):
    highest = lax.Precision.HIGH
    count, index = (lax.axis_size(axis), lax.axis_index(axis))
    pair_count = lax.axis_size(pair_axis)
    side = lax.axis_index(pair_axis) % 2
    width = matrix.shape[1] // 2
    swap = [(j, j ^ 1) for j in range(pair_count)]
    mine = lax.dynamic_slice_in_dim(matrix, side * width, width, axis=1)
    distance = 1
    while distance < count:
        pairs = [(j, j + distance) for j in range(count - distance)]
        last = 2 * distance >= count
        has = index >= distance
        got_vector = lax.ppermute(vector, axis, pairs)
        if not last:
            got_half = lax.ppermute(mine, axis, pairs)
        newer = jnp.einsum("sq,rq->sr", got_vector, matrix, precision=highest) + vector
        vector = jnp.where(has, newer, vector)
        if not last:
            own = jnp.dot(matrix, got_half, precision=highest)
            other = lax.ppermute(own, pair_axis, swap)
            joined = jnp.where(
                side == 0,
                jnp.concatenate([own, other], axis=1),
                jnp.concatenate([other, own], axis=1),
            )
            matrix = jnp.where(has, joined, matrix)
            mine = jnp.where(has, own, mine)
        distance = distance * 2
    return vector


def on_device_body(tm_groups, operators, input_maps, segment, load, initial, observed):
    highest = lax.Precision.HIGHEST
    step_count = operators.shape[0]
    modes = operators.shape[1]
    local_scen = initial.shape[0]
    time_shards = lax.axis_size("tm")
    scen_shards = lax.axis_size("scen")
    regimes = jnp.arange(input_maps.shape[0], dtype=jnp.int32)
    onehot = (segment[:, None] == regimes[None, :]).astype(jnp.bfloat16)
    weighted = jnp.einsum(
        "tg,grk->trk", onehot, input_maps, preferred_element_type=jnp.float32
    ).astype(jnp.bfloat16)
    forcing = jnp.einsum("tsk,trk->tsr", load, weighted, preferred_element_type=jnp.float32)
    first_shard = lax.axis_index("tm") == 0
    anchor = jnp.where(first_shard, initial, jnp.zeros_like(initial))

    def advance(current, inputs):
        matrix, heating = inputs
        updated = jnp.einsum("sq,rq->sr", current, matrix, precision=highest) + heating
        return (updated, updated)

    last_state, local_states = lax.scan(advance, anchor, (operators, forcing))
    identity_matrix = jnp.eye(modes, dtype=jnp.float32)

    def compose_step(product, matrix):
        newer = jnp.dot(matrix, product, precision=highest)
        return (newer, newer)

    if step_count == 1:
        composed, products = (operators[0], operators)
    else:
        composed, products = lax.scan(compose_step, identity_matrix, operators)
    composed = jnp.where(first_shard, jnp.zeros_like(composed), composed)
    leaving = shift_scan(composed, last_state, "tm", "scen")
    if step_count == 1:
        states = leaving[None]
    else:
        pairs = [(j, j + 1) for j in range(time_shards - 1)]
        entering = lax.ppermute(leaving, "tm", pairs)
        states = local_states + jnp.einsum("sq,trq->tsr", entering, products, precision=highest)
    normalize = 1.0 / (step_count * time_shards * local_scen * scen_shards)
    sensors = observed.shape[2]
    cross_cols = sensors // scen_shards
    gram_cols = modes // scen_shards
    readings = observed.astype(jnp.float32).reshape(step_count * local_scen, scen_shards, cross_cols)
    readings = lax.all_to_all(readings, "scen", 1, 0, tiled=True)
    readings = readings.reshape(scen_shards, step_count, local_scen, cross_cols)
    readings = readings.transpose(1, 0, 2, 3).reshape(step_count, scen_shards * local_scen, cross_cols)
    every = lax.all_to_all(
        jnp.broadcast_to(states[None], (scen_shards,) + states.shape), "scen", 0, 0, tiled=True
    )
    every = every.reshape(scen_shards, step_count, local_scen, modes).transpose(1, 0, 2, 3)
    every = every.reshape(step_count, scen_shards * local_scen, modes)
    column = lax.axis_index("scen") * gram_cols
    right = jnp.concatenate(
        [lax.dynamic_slice_in_dim(every, column, gram_cols, axis=2), readings], axis=2
    )
    joined = jnp.einsum("tsr,tso->ro", every, right, precision=highest) * normalize
    mine = joined
    stride = time_shards
    for size in tm_groups:
        stride //= size
        groups = [
            [base + k * stride for k in range(size)]
            for base in range(time_shards)
            if (base // stride) % size == 0
        ]
        pieces = mine.reshape(size, mine.shape[0] // size, mine.shape[1])
        mine = lax.all_to_all(pieces, "tm", 0, 0, tiled=True, axis_index_groups=groups).sum(axis=0)
    return (states, mine[:, :gram_cols], mine[:, gram_cols:])


def solution(mesh):
    in_specs = (
        P("tm", None, None),
        P(),
        P("tm"),
        P("tm", "scen", None),
        P("scen", None),
        P("tm", "scen", None),
    )
    out_specs = (P("tm", "scen", None), P("tm", "scen"), P("tm", "scen"))
    count = dict(zip(mesh.axis_names, mesh.devices.shape))["tm"]
    tm_groups = (count // 8, 8) if count % 8 == 0 and count > 8 else (count,)

    def on_device(*args):
        return on_device_body(tm_groups, *args)

    return jax.shard_map(
        on_device, mesh=mesh, in_specs=in_specs, out_specs=out_specs, check_vma=False
    )
```

```python
import jax
import jax.numpy as jnp
from jax import lax
from jax.sharding import PartitionSpec as P


def shift_scan(matrix, vector, axis, pair_axis):
    highest = lax.Precision.HIGHEST
    count, index = (lax.axis_size(axis), lax.axis_index(axis))
    pair_count = lax.axis_size(pair_axis)
    side = lax.axis_index(pair_axis) % 2
    width = matrix.shape[1] // 2
    swap = [(j, j ^ 1) for j in range(pair_count)]
    mine = lax.dynamic_slice_in_dim(matrix, side * width, width, axis=1)
    distance = 1
    while distance < count:
        pairs = [(j, j + distance) for j in range(count - distance)]
        last = 2 * distance >= count
        has = index >= distance
        got_vector = lax.ppermute(vector, axis, pairs)
        if not last:
            got_half = lax.ppermute(mine, axis, pairs)
        newer = jnp.einsum("sq,rq->sr", got_vector, matrix, precision=highest) + vector
        vector = jnp.where(has, newer, vector)
        if not last:
            own = jnp.dot(matrix, got_half, precision=highest)
            other = lax.ppermute(own, pair_axis, swap)
            joined = jnp.where(
                side == 0,
                jnp.concatenate([own, other], axis=1),
                jnp.concatenate([other, own], axis=1),
            )
            matrix = jnp.where(has, joined, matrix)
            mine = jnp.where(has, own, mine)
        distance = distance * 2
    return vector


def on_device_body(tm_groups, operators, input_maps, segment, load, initial, observed):
    highest = lax.Precision.HIGHEST
    step_count = operators.shape[0]
    modes = operators.shape[1]
    local_scen = initial.shape[0]
    time_shards = lax.axis_size("tm")
    scen_shards = lax.axis_size("scen")
    regimes = jnp.arange(input_maps.shape[0], dtype=jnp.int32)
    onehot = (segment[:, None] == regimes[None, :]).astype(jnp.bfloat16)
    weighted = jnp.einsum(
        "tg,grk->trk", onehot, input_maps, preferred_element_type=jnp.float32
    ).astype(jnp.bfloat16)
    forcing = jnp.einsum("tsk,trk->tsr", load, weighted, preferred_element_type=jnp.float32)
    first_shard = lax.axis_index("tm") == 0
    anchor = jnp.where(first_shard, initial, jnp.zeros_like(initial))

    def advance(current, inputs):
        matrix, heating = inputs
        updated = jnp.einsum("sq,rq->sr", current, matrix, precision=highest) + heating
        return (updated, updated)

    last_state, local_states = lax.scan(advance, anchor, (operators, forcing))
    identity_matrix = jnp.eye(modes, dtype=jnp.float32)

    def compose_step(product, matrix):
        newer = jnp.dot(matrix, product, precision=highest)
        return (newer, newer)

    if step_count == 1:
        composed, products = (operators[0], operators)
    else:
        composed, products = lax.scan(compose_step, identity_matrix, operators)
    composed = jnp.where(first_shard, jnp.zeros_like(composed), composed)
    leaving = shift_scan(composed, last_state, "tm", "scen")
    if step_count == 1:
        states = leaving[None]
    else:
        pairs = [(j, j + 1) for j in range(time_shards - 1)]
        entering = lax.ppermute(leaving, "tm", pairs)
        states = local_states + jnp.einsum("sq,trq->tsr", entering, products, precision=highest)
    normalize = 1.0 / (step_count * time_shards * local_scen * scen_shards)
    sensors = observed.shape[2]
    cross_cols = sensors // scen_shards
    gram_cols = modes // scen_shards
    readings = observed.astype(jnp.float32).reshape(step_count * local_scen, scen_shards, cross_cols)
    readings = lax.all_to_all(readings, "scen", 1, 0, tiled=True)
    readings = readings.reshape(scen_shards, step_count, local_scen, cross_cols)
    readings = readings.transpose(1, 0, 2, 3).reshape(step_count, scen_shards * local_scen, cross_cols)
    core = lax.axis_index("scen") % 2
    partner = lax.ppermute(states, "scen", [(j, j ^ 1) for j in range(scen_shards)])
    pair = jnp.where(
        core == 0,
        jnp.concatenate([states, partner], axis=1),
        jnp.concatenate([partner, states], axis=1),
    )
    chips = scen_shards // 2
    groups = [[c + 2 * k for k in range(chips)] for c in range(2)]
    every = lax.all_to_all(
        jnp.broadcast_to(pair[None], (chips,) + pair.shape),
        "scen", 0, 0, tiled=True, axis_index_groups=groups,
    )
    every = every.reshape(chips, step_count, 2 * local_scen, modes).transpose(1, 0, 2, 3)
    every = every.reshape(step_count, scen_shards * local_scen, modes)
    column = lax.axis_index("scen") * gram_cols
    right = jnp.concatenate(
        [lax.dynamic_slice_in_dim(every, column, gram_cols, axis=2), readings], axis=2
    )
    joined = jnp.einsum("tsr,tso->ro", every, right, precision=highest) * normalize
    mine = joined
    stride = time_shards
    for size in tm_groups:
        stride //= size
        groups = [
            [base + k * stride for k in range(size)]
            for base in range(time_shards)
            if (base // stride) % size == 0
        ]
        pieces = mine.reshape(size, mine.shape[0] // size, mine.shape[1])
        mine = lax.all_to_all(pieces, "tm", 0, 0, tiled=True, axis_index_groups=groups).sum(axis=0)
    return (states, mine[:, :gram_cols], mine[:, gram_cols:])


def solution(mesh):
    in_specs = (
        P("tm", None, None),
        P(),
        P("tm"),
        P("tm", "scen", None),
        P("scen", None),
        P("tm", "scen", None),
    )
    out_specs = (P("tm", "scen", None), P("tm", "scen"), P("tm", "scen"))
    count = dict(zip(mesh.axis_names, mesh.devices.shape))["tm"]
    tm_groups = (count // 8, 8) if count % 8 == 0 and count > 8 else (count,)

    def on_device(*args):
        return on_device_body(tm_groups, *args)

    return jax.shard_map(
        on_device, mesh=mesh, in_specs=in_specs, out_specs=out_specs, check_vma=False
    )
```

```python
import jax
import jax.numpy as jnp
from jax import lax
from jax.sharding import PartitionSpec as P


def shift_scan(matrix, vector, axis, pair_axis):
    highest = lax.Precision.HIGHEST
    count, index = (lax.axis_size(axis), lax.axis_index(axis))
    pair_count = lax.axis_size(pair_axis)
    part = lax.axis_index(pair_axis) % 4
    width = matrix.shape[1] // 4
    across = [(j, j ^ 2) for j in range(pair_count)]
    swap = [(j, j ^ 1) for j in range(pair_count)]
    place = jnp.array([0, 2, 1, 3], jnp.int32)[part ^ jnp.arange(4, dtype=jnp.int32)]
    mine = lax.dynamic_slice_in_dim(matrix, part * width, width, axis=1)
    distance = 1
    while distance < count:
        pairs = [(j, j + distance) for j in range(count - distance)]
        last = 2 * distance >= count
        has = index >= distance
        got_vector = lax.ppermute(vector, axis, pairs)
        if not last:
            got_part = lax.ppermute(mine, axis, pairs)
        newer = jnp.einsum("sq,rq->sr", got_vector, matrix, precision=highest) + vector
        vector = jnp.where(has, newer, vector)
        if not last:
            own = jnp.dot(matrix, got_part, precision=highest)
            far = lax.ppermute(own, pair_axis, across)
            near = lax.ppermute(jnp.stack([own, far]), pair_axis, swap)
            pieces = jnp.concatenate([jnp.stack([own, far]), near], axis=0)
            ordered = jnp.take(pieces, place, axis=0)
            joined = jnp.concatenate([ordered[k] for k in range(4)], axis=1)
            matrix = jnp.where(has, joined, matrix)
            mine = jnp.where(has, own, mine)
        distance = distance * 2
    return vector


def on_device_body(tm_groups, operators, input_maps, segment, load, initial, observed):
    highest = lax.Precision.HIGHEST
    step_count = operators.shape[0]
    modes = operators.shape[1]
    local_scen = initial.shape[0]
    time_shards = lax.axis_size("tm")
    scen_shards = lax.axis_size("scen")
    regimes = jnp.arange(input_maps.shape[0], dtype=jnp.int32)
    onehot = (segment[:, None] == regimes[None, :]).astype(jnp.bfloat16)
    weighted = jnp.einsum(
        "tg,grk->trk", onehot, input_maps, preferred_element_type=jnp.float32
    ).astype(jnp.bfloat16)
    forcing = jnp.einsum("tsk,trk->tsr", load, weighted, preferred_element_type=jnp.float32)
    first_shard = lax.axis_index("tm") == 0
    anchor = jnp.where(first_shard, initial, jnp.zeros_like(initial))

    def advance(current, inputs):
        matrix, heating = inputs
        updated = jnp.einsum("sq,rq->sr", current, matrix, precision=highest) + heating
        return (updated, updated)

    last_state, local_states = lax.scan(advance, anchor, (operators, forcing))
    identity_matrix = jnp.eye(modes, dtype=jnp.float32)

    def compose_step(product, matrix):
        newer = jnp.dot(matrix, product, precision=highest)
        return (newer, newer)

    if step_count == 1:
        composed, products = (operators[0], operators)
    else:
        composed, products = lax.scan(compose_step, identity_matrix, operators)
    composed = jnp.where(first_shard, jnp.zeros_like(composed), composed)
    leaving = shift_scan(composed, last_state, "tm", "scen")
    if step_count == 1:
        states = leaving[None]
    else:
        pairs = [(j, j + 1) for j in range(time_shards - 1)]
        entering = lax.ppermute(leaving, "tm", pairs)
        states = local_states + jnp.einsum("sq,trq->tsr", entering, products, precision=highest)
    normalize = 1.0 / (step_count * time_shards * local_scen * scen_shards)
    sensors = observed.shape[2]
    cross_cols = sensors // scen_shards
    gram_cols = modes // scen_shards
    readings = observed.astype(jnp.float32).reshape(step_count * local_scen, scen_shards, cross_cols)
    readings = lax.all_to_all(readings, "scen", 1, 0, tiled=True)
    readings = readings.reshape(scen_shards, step_count, local_scen, cross_cols)
    readings = readings.transpose(1, 0, 2, 3).reshape(step_count, scen_shards * local_scen, cross_cols)
    core = lax.axis_index("scen") % 2
    partner = lax.ppermute(states, "scen", [(j, j ^ 1) for j in range(scen_shards)])
    pair = jnp.where(
        core == 0,
        jnp.concatenate([states, partner], axis=1),
        jnp.concatenate([partner, states], axis=1),
    )
    chips = scen_shards // 2
    groups = [[c + 2 * k for k in range(chips)] for c in range(2)]
    every = lax.all_to_all(
        jnp.broadcast_to(pair[None], (chips,) + pair.shape),
        "scen", 0, 0, tiled=True, axis_index_groups=groups,
    )
    every = every.reshape(chips, step_count, 2 * local_scen, modes).transpose(1, 0, 2, 3)
    every = every.reshape(step_count, scen_shards * local_scen, modes)
    column = lax.axis_index("scen") * gram_cols
    right = jnp.concatenate(
        [lax.dynamic_slice_in_dim(every, column, gram_cols, axis=2), readings], axis=2
    )
    joined = jnp.einsum("tsr,tso->ro", every, right, precision=highest) * normalize
    mine = joined
    stride = time_shards
    for size in tm_groups:
        stride //= size
        groups = [
            [base + k * stride for k in range(size)]
            for base in range(time_shards)
            if (base // stride) % size == 0
        ]
        pieces = mine.reshape(size, mine.shape[0] // size, mine.shape[1])
        mine = lax.all_to_all(pieces, "tm", 0, 0, tiled=True, axis_index_groups=groups).sum(axis=0)
    return (states, mine[:, :gram_cols], mine[:, gram_cols:])


def solution(mesh):
    in_specs = (
        P("tm", None, None),
        P(),
        P("tm"),
        P("tm", "scen", None),
        P("scen", None),
        P("tm", "scen", None),
    )
    out_specs = (P("tm", "scen", None), P("tm", "scen"), P("tm", "scen"))
    count = dict(zip(mesh.axis_names, mesh.devices.shape))["tm"]
    tm_groups = (count // 8, 8) if count % 8 == 0 and count > 8 else (count,)

    def on_device(*args):
        return on_device_body(tm_groups, *args)

    return jax.shard_map(
        on_device, mesh=mesh, in_specs=in_specs, out_specs=out_specs, check_vma=False
    )
```

```python
import jax
import jax.numpy as jnp
from jax import lax
from jax.sharding import PartitionSpec as P


def shift_scan(matrix, vector, axis, pair_axis):
    highest = lax.Precision.HIGHEST
    count, index = (lax.axis_size(axis), lax.axis_index(axis))
    pair_count = lax.axis_size(pair_axis)
    part = lax.axis_index(pair_axis) % 4
    width = matrix.shape[1] // 4
    across = [(j, j ^ 2) for j in range(pair_count)]
    swap = [(j, j ^ 1) for j in range(pair_count)]
    place = jnp.array([0, 2, 1, 3], jnp.int32)[part ^ jnp.arange(4, dtype=jnp.int32)]
    mine = lax.dynamic_slice_in_dim(matrix, part * width, width, axis=1)
    distance = 1
    while distance < count:
        pairs = [(j, j + distance) for j in range(count - distance)]
        last = 2 * distance >= count
        has = index >= distance
        got_vector = lax.ppermute(vector, axis, pairs)
        if not last:
            got_part = lax.ppermute(mine, axis, pairs)
        newer = jnp.einsum("sq,rq->sr", got_vector, matrix, precision=highest) + vector
        vector = jnp.where(has, newer, vector)
        if not last:
            own = jnp.dot(matrix, got_part, precision=highest)
            far = lax.ppermute(own, pair_axis, across)
            near = lax.ppermute(jnp.stack([own, far]), pair_axis, swap)
            pieces = jnp.concatenate([jnp.stack([own, far]), near], axis=0)
            ordered = jnp.take(pieces, place, axis=0)
            joined = jnp.concatenate([ordered[k] for k in range(4)], axis=1)
            matrix = jnp.where(has, joined, matrix)
            mine = jnp.where(has, own, mine)
        distance = distance * 2
    return vector


def on_device_body(tm_groups, operators, input_maps, segment, load, initial, observed):
    highest = lax.Precision.HIGHEST
    step_count = operators.shape[0]
    modes = operators.shape[1]
    local_scen = initial.shape[0]
    time_shards = lax.axis_size("tm")
    scen_shards = lax.axis_size("scen")
    regimes = jnp.arange(input_maps.shape[0], dtype=jnp.int32)
    onehot = (segment[:, None] == regimes[None, :]).astype(jnp.bfloat16)
    weighted = jnp.einsum(
        "tg,grk->trk", onehot, input_maps, preferred_element_type=jnp.float32
    ).astype(jnp.bfloat16)
    forcing = jnp.einsum("tsk,trk->tsr", load, weighted, preferred_element_type=jnp.float32)
    first_shard = lax.axis_index("tm") == 0
    anchor = jnp.where(first_shard, initial, jnp.zeros_like(initial))

    def advance(current, inputs):
        matrix, heating = inputs
        updated = jnp.einsum("sq,rq->sr", current, matrix, precision=highest) + heating
        return (updated, updated)

    last_state, local_states = lax.scan(advance, anchor, (operators, forcing))
    identity_matrix = jnp.eye(modes, dtype=jnp.float32)

    def compose_step(product, matrix):
        newer = jnp.dot(matrix, product, precision=highest)
        return (newer, newer)

    if step_count == 1:
        composed, products = (operators[0], operators)
    else:
        composed, products = lax.scan(compose_step, identity_matrix, operators)
    composed = jnp.where(first_shard, jnp.zeros_like(composed), composed)
    leaving = shift_scan(composed, last_state, "tm", "scen")
    if step_count == 1:
        states = leaving[None]
    else:
        pairs = [(j, j + 1) for j in range(time_shards - 1)]
        entering = lax.ppermute(leaving, "tm", pairs)
        states = local_states + jnp.einsum("sq,trq->tsr", entering, products, precision=highest)
    normalize = 1.0 / (step_count * time_shards * local_scen * scen_shards)
    sensors = observed.shape[2]
    cross_cols = sensors // scen_shards
    gram_cols = modes // scen_shards
    readings = observed.astype(jnp.float32).reshape(step_count, local_scen, scen_shards, cross_cols)
    readings = readings.transpose(2, 0, 1, 3)
    payload = jnp.concatenate(
        [jnp.broadcast_to(states[None], (scen_shards,) + states.shape), readings], axis=3
    )
    received = lax.all_to_all(payload, "scen", 0, 0, tiled=True)
    received = received.reshape(scen_shards, step_count, local_scen, modes + cross_cols)
    received = received.transpose(1, 0, 2, 3).reshape(
        step_count, scen_shards * local_scen, modes + cross_cols
    )
    every = received[:, :, :modes]
    readings = received[:, :, modes:]
    column = lax.axis_index("scen") * gram_cols
    right = jnp.concatenate(
        [lax.dynamic_slice_in_dim(every, column, gram_cols, axis=2), readings], axis=2
    )
    joined = jnp.einsum("tsr,tso->ro", every, right, precision=highest) * normalize
    mine = joined
    stride = time_shards
    for size in tm_groups:
        stride //= size
        groups = [
            [base + k * stride for k in range(size)]
            for base in range(time_shards)
            if (base // stride) % size == 0
        ]
        pieces = mine.reshape(size, mine.shape[0] // size, mine.shape[1])
        mine = lax.all_to_all(pieces, "tm", 0, 0, tiled=True, axis_index_groups=groups).sum(axis=0)
    return (states, mine[:, :gram_cols], mine[:, gram_cols:])


def solution(mesh):
    in_specs = (
        P("tm", None, None),
        P(),
        P("tm"),
        P("tm", "scen", None),
        P("scen", None),
        P("tm", "scen", None),
    )
    out_specs = (P("tm", "scen", None), P("tm", "scen"), P("tm", "scen"))
    count = dict(zip(mesh.axis_names, mesh.devices.shape))["tm"]
    tm_groups = (count // 8, 8) if count % 8 == 0 and count > 8 else (count,)

    def on_device(*args):
        return on_device_body(tm_groups, *args)

    return jax.shard_map(
        on_device, mesh=mesh, in_specs=in_specs, out_specs=out_specs, check_vma=False
    )
```

```python
import jax
import jax.numpy as jnp
from jax import lax
from jax.sharding import PartitionSpec as P


def shift_scan(matrix, vector, axis, pair_axis):
    highest = lax.Precision.HIGHEST
    count = lax.axis_size(axis)
    pair_count = lax.axis_size(pair_axis)
    part = lax.axis_index(pair_axis) % 4
    width = matrix.shape[1] // 4
    across = [(j, j ^ 2) for j in range(pair_count)]
    swap = [(j, j ^ 1) for j in range(pair_count)]
    quarters = [part, part ^ 2, part ^ 1, part ^ 3]
    pieces = [lax.dynamic_slice_in_dim(matrix, k * width, width, axis=1) for k in quarters]
    distance = 1
    while distance < count:
        pairs = [(j, j + distance) for j in range(count - distance)]
        last = 2 * distance >= count
        got_vector = lax.ppermute(vector, axis, pairs)
        if not last:
            got_part = lax.ppermute(pieces[0], axis, pairs)
        newer = vector
        for piece, k in zip(pieces, quarters):
            front = lax.dynamic_slice_in_dim(got_vector, k * width, width, axis=1)
            newer = newer + jnp.einsum("sq,rq->sr", front, piece, precision=highest)
        vector = newer
        if not last:
            own = None
            for piece, k in zip(pieces, quarters):
                block = lax.dynamic_slice_in_dim(got_part, k * width, width, axis=0)
                term = jnp.dot(piece, block, precision=highest)
                own = term if own is None else own + term
            far = lax.ppermute(own, pair_axis, across)
            near = lax.ppermute(jnp.stack([own, far]), pair_axis, swap)
            pieces = [own, far, near[0], near[1]]
        distance = distance * 2
    return vector


def on_device_body(tm_groups, operators, input_maps, segment, load, initial, observed):
    highest = lax.Precision.HIGHEST
    step_count = operators.shape[0]
    modes = operators.shape[1]
    local_scen = initial.shape[0]
    time_shards = lax.axis_size("tm")
    scen_shards = lax.axis_size("scen")
    regimes = jnp.arange(input_maps.shape[0], dtype=jnp.int32)
    onehot = (segment[:, None] == regimes[None, :]).astype(jnp.bfloat16)
    weighted = jnp.einsum(
        "tg,grk->trk", onehot, input_maps, preferred_element_type=jnp.float32
    ).astype(jnp.bfloat16)
    forcing = jnp.einsum("tsk,trk->tsr", load, weighted, preferred_element_type=jnp.float32)
    first_shard = lax.axis_index("tm") == 0
    anchor = jnp.where(first_shard, initial, jnp.zeros_like(initial))

    def advance(current, inputs):
        matrix, heating = inputs
        updated = jnp.einsum("sq,rq->sr", current, matrix, precision=highest) + heating
        return (updated, updated)

    last_state, local_states = lax.scan(advance, anchor, (operators, forcing))
    identity_matrix = jnp.eye(modes, dtype=jnp.float32)

    def compose_step(product, matrix):
        newer = jnp.dot(matrix, product, precision=highest)
        return (newer, newer)

    if step_count == 1:
        composed, products = (operators[0], operators)
    else:
        composed, products = lax.scan(compose_step, identity_matrix, operators)
    composed = jnp.where(first_shard, jnp.zeros_like(composed), composed)
    leaving = shift_scan(composed, last_state, "tm", "scen")
    if step_count == 1:
        states = leaving[None]
    else:
        pairs = [(j, j + 1) for j in range(time_shards - 1)]
        entering = lax.ppermute(leaving, "tm", pairs)
        states = local_states + jnp.einsum("sq,trq->tsr", entering, products, precision=highest)
    normalize = 1.0 / (step_count * time_shards * local_scen * scen_shards)
    sensors = observed.shape[2]
    cross_cols = sensors // scen_shards
    gram_cols = modes // scen_shards
    readings = observed.astype(jnp.float32).reshape(step_count, local_scen, scen_shards, cross_cols)
    readings = readings.transpose(2, 0, 1, 3)
    payload = jnp.concatenate(
        [jnp.broadcast_to(states[None], (scen_shards,) + states.shape), readings], axis=3
    )
    received = lax.all_to_all(payload, "scen", 0, 0, tiled=True)
    received = received.reshape(scen_shards, step_count, local_scen, modes + cross_cols)
    received = received.transpose(1, 0, 2, 3).reshape(
        step_count, scen_shards * local_scen, modes + cross_cols
    )
    every = received[:, :, :modes]
    readings = received[:, :, modes:]
    column = lax.axis_index("scen") * gram_cols
    right = jnp.concatenate(
        [lax.dynamic_slice_in_dim(every, column, gram_cols, axis=2), readings], axis=2
    )
    joined = jnp.einsum("tsr,tso->ro", every, right, precision=highest) * normalize
    outer, inner = tm_groups if len(tm_groups) == 2 else (1, time_shards)
    block = modes // time_shards
    pieces = joined.reshape(outer, inner, block, joined.shape[1]).transpose(1, 0, 2, 3)
    near_groups = [[base * inner + k for k in range(inner)] for base in range(outer)]
    pieces = lax.all_to_all(pieces, "tm", 0, 0, tiled=True, axis_index_groups=near_groups)
    mine = pieces.reshape(inner, outer, block, joined.shape[1]).sum(axis=0)
    if outer > 1:
        far_groups = [[k * inner + base for k in range(outer)] for base in range(inner)]
        mine = lax.all_to_all(mine, "tm", 0, 0, tiled=True, axis_index_groups=far_groups)
        mine = mine.sum(axis=0)
    else:
        mine = mine[0]
    return (states, mine[:, :gram_cols], mine[:, gram_cols:])


def solution(mesh):
    in_specs = (
        P("tm", None, None),
        P(),
        P("tm"),
        P("tm", "scen", None),
        P("scen", None),
        P("tm", "scen", None),
    )
    out_specs = (P("tm", "scen", None), P("tm", "scen"), P("tm", "scen"))
    count = dict(zip(mesh.axis_names, mesh.devices.shape))["tm"]
    tm_groups = (count // 8, 8) if count % 8 == 0 and count > 8 else (count,)

    def on_device(*args):
        return on_device_body(tm_groups, *args)

    return jax.shard_map(
        on_device, mesh=mesh, in_specs=in_specs, out_specs=out_specs, check_vma=False
    )
```

```python
import jax
import jax.numpy as jnp
from jax import lax
from jax.sharding import PartitionSpec as P


def shift_scan(matrix, vector, axis, pair_axis):
    highest = lax.Precision.HIGHEST
    count = lax.axis_size(axis)
    pair_count = lax.axis_size(pair_axis)
    part = lax.axis_index(pair_axis) % 4
    width = matrix.shape[1] // 4
    across = [(j, j ^ 2) for j in range(pair_count)]
    swap = [(j, j ^ 1) for j in range(pair_count)]
    quarters = [part, part ^ 2, part ^ 1, part ^ 3]
    pieces = [lax.dynamic_slice_in_dim(matrix, k * width, width, axis=1) for k in quarters]
    distance = 1
    while distance < count:
        pairs = [(j, j + distance) for j in range(count - distance)]
        last = 2 * distance >= count
        got_vector = lax.ppermute(vector, axis, pairs)
        if not last:
            got_part = lax.ppermute(pieces[0], axis, pairs)
        newer = vector
        for piece, k in zip(pieces, quarters):
            front = lax.dynamic_slice_in_dim(got_vector, k * width, width, axis=1)
            newer = newer + jnp.einsum("sq,rq->sr", front, piece, precision=highest)
        vector = newer
        if not last:
            own = None
            for piece, k in zip(pieces, quarters):
                block = lax.dynamic_slice_in_dim(got_part, k * width, width, axis=0)
                term = jnp.dot(piece, block, precision=highest)
                own = term if own is None else own + term
            far = lax.ppermute(own, pair_axis, across)
            near = lax.ppermute(jnp.stack([own, far]), pair_axis, swap)
            pieces = [own, far, near[0], near[1]]
        distance = distance * 2
    return vector


def on_device_body(tm_groups, operators, input_maps, segment, load, initial, observed):
    highest = lax.Precision.HIGHEST
    step_count = operators.shape[0]
    modes = operators.shape[1]
    local_scen = initial.shape[0]
    time_shards = lax.axis_size("tm")
    scen_shards = lax.axis_size("scen")
    regimes = jnp.arange(input_maps.shape[0], dtype=jnp.int32)
    onehot = (segment[:, None] == regimes[None, :]).astype(jnp.bfloat16)
    weighted = jnp.einsum(
        "tg,grk->trk", onehot, input_maps, preferred_element_type=jnp.float32
    ).astype(jnp.bfloat16)
    forcing = jnp.einsum("tsk,trk->tsr", load, weighted, preferred_element_type=jnp.float32)
    first_shard = lax.axis_index("tm") == 0
    anchor = jnp.where(first_shard, initial, jnp.zeros_like(initial))

    def advance(current, inputs):
        matrix, heating = inputs
        updated = jnp.einsum("sq,rq->sr", current, matrix, precision=highest) + heating
        return (updated, updated)

    last_state, local_states = lax.scan(advance, anchor, (operators, forcing))
    identity_matrix = jnp.eye(modes, dtype=jnp.float32)

    def compose_step(product, matrix):
        newer = jnp.dot(matrix, product, precision=highest)
        return (newer, newer)

    if step_count == 1:
        composed, products = (operators[0], operators)
    else:
        composed, products = lax.scan(compose_step, identity_matrix, operators)
    composed = jnp.where(first_shard, jnp.zeros_like(composed), composed)
    leaving = shift_scan(composed, last_state, "tm", "scen")
    if step_count == 1:
        states = leaving[None]
    else:
        pairs = [(j, j + 1) for j in range(time_shards - 1)]
        entering = lax.ppermute(leaving, "tm", pairs)
        states = local_states + jnp.einsum("sq,trq->tsr", entering, products, precision=highest)
    normalize = 1.0 / (step_count * time_shards * local_scen * scen_shards)
    sensors = observed.shape[2]
    cross_cols = sensors // scen_shards
    gram_cols = modes // scen_shards
    readings = observed.astype(jnp.float32).reshape(step_count * local_scen, scen_shards, cross_cols)
    readings = lax.all_to_all(readings, "scen", 1, 0, tiled=True)
    readings = readings.reshape(scen_shards, step_count, local_scen, cross_cols)
    readings = readings.transpose(1, 0, 2, 3).reshape(step_count, scen_shards * local_scen, cross_cols)
    every = lax.all_to_all(
        jnp.broadcast_to(states[None], (scen_shards,) + states.shape), "scen", 0, 0, tiled=True
    )
    every = every.reshape(scen_shards, step_count, local_scen, modes).transpose(1, 0, 2, 3)
    every = every.reshape(step_count, scen_shards * local_scen, modes)
    column = lax.axis_index("scen") * gram_cols
    right = jnp.concatenate(
        [lax.dynamic_slice_in_dim(every, column, gram_cols, axis=2), readings], axis=2
    )
    joined = jnp.einsum("tsr,tso->ro", every, right, precision=highest) * normalize
    mine = joined
    stride = time_shards
    for size in tm_groups:
        stride //= size
        groups = [
            [base + k * stride for k in range(size)]
            for base in range(time_shards)
            if (base // stride) % size == 0
        ]
        pieces = mine.reshape(size, mine.shape[0] // size, mine.shape[1])
        mine = lax.all_to_all(pieces, "tm", 0, 0, tiled=True, axis_index_groups=groups).sum(axis=0)
    return (states, mine[:, :gram_cols], mine[:, gram_cols:])


def solution(mesh):
    in_specs = (
        P("tm", None, None),
        P(),
        P("tm"),
        P("tm", "scen", None),
        P("scen", None),
        P("tm", "scen", None),
    )
    out_specs = (P("tm", "scen", None), P("tm", "scen"), P("tm", "scen"))
    count = dict(zip(mesh.axis_names, mesh.devices.shape))["tm"]
    tm_groups = (count // 8, 8) if count % 8 == 0 and count > 8 else (count,)

    def on_device(*args):
        return on_device_body(tm_groups, *args)

    return jax.shard_map(
        on_device, mesh=mesh, in_specs=in_specs, out_specs=out_specs, check_vma=False
    )
```

```python
import jax
import jax.numpy as jnp
from jax import lax
from jax.sharding import PartitionSpec as P


def shift_scan(matrix, vector, axis, pair_axis):
    highest = lax.Precision.HIGHEST
    count = lax.axis_size(axis)
    pair_count = lax.axis_size(pair_axis)
    part = lax.axis_index(pair_axis) % 4
    width = matrix.shape[1] // 4
    across = [(j, j ^ 2) for j in range(pair_count)]
    swap = [(j, j ^ 1) for j in range(pair_count)]
    quarters = [part, part ^ 2, part ^ 1, part ^ 3]
    pieces = [lax.dynamic_slice_in_dim(matrix, k * width, width, axis=1) for k in quarters]
    distance = 1
    while distance < count:
        pairs = [(j, j + distance) for j in range(count - distance)]
        last = 2 * distance >= count
        got_vector = lax.ppermute(vector, axis, pairs)
        if not last:
            got_part = lax.ppermute(pieces[0], axis, pairs)
        newer = vector
        for piece, k in zip(pieces, quarters):
            front = lax.dynamic_slice_in_dim(got_vector, k * width, width, axis=1)
            newer = newer + jnp.einsum("sq,rq->sr", front, piece, precision=highest)
        vector = newer
        if not last:
            own = None
            for piece, k in zip(pieces, quarters):
                block = lax.dynamic_slice_in_dim(got_part, k * width, width, axis=0)
                term = jnp.dot(piece, block, precision=lax.Precision.HIGH)
                own = term if own is None else own + term
            far = lax.ppermute(own, pair_axis, across)
            near = lax.ppermute(jnp.stack([own, far]), pair_axis, swap)
            pieces = [own, far, near[0], near[1]]
        distance = distance * 2
    return vector


def on_device_body(tm_groups, operators, input_maps, segment, load, initial, observed):
    highest = lax.Precision.HIGHEST
    step_count = operators.shape[0]
    modes = operators.shape[1]
    local_scen = initial.shape[0]
    time_shards = lax.axis_size("tm")
    scen_shards = lax.axis_size("scen")
    regimes = jnp.arange(input_maps.shape[0], dtype=jnp.int32)
    onehot = (segment[:, None] == regimes[None, :]).astype(jnp.bfloat16)
    weighted = jnp.einsum(
        "tg,grk->trk", onehot, input_maps, preferred_element_type=jnp.float32
    ).astype(jnp.bfloat16)
    forcing = jnp.einsum("tsk,trk->tsr", load, weighted, preferred_element_type=jnp.float32)
    first_shard = lax.axis_index("tm") == 0
    anchor = jnp.where(first_shard, initial, jnp.zeros_like(initial))

    def advance(current, inputs):
        matrix, heating = inputs
        updated = jnp.einsum("sq,rq->sr", current, matrix, precision=highest) + heating
        return (updated, updated)

    last_state, local_states = lax.scan(advance, anchor, (operators, forcing))
    identity_matrix = jnp.eye(modes, dtype=jnp.float32)

    def compose_step(product, matrix):
        newer = jnp.dot(matrix, product, precision=highest)
        return (newer, newer)

    if step_count == 1:
        composed, products = (operators[0], operators)
    else:
        composed, products = lax.scan(compose_step, identity_matrix, operators)
    composed = jnp.where(first_shard, jnp.zeros_like(composed), composed)
    leaving = shift_scan(composed, last_state, "tm", "scen")
    if step_count == 1:
        states = leaving[None]
    else:
        pairs = [(j, j + 1) for j in range(time_shards - 1)]
        entering = lax.ppermute(leaving, "tm", pairs)
        states = local_states + jnp.einsum("sq,trq->tsr", entering, products, precision=highest)
    normalize = 1.0 / (step_count * time_shards * local_scen * scen_shards)
    sensors = observed.shape[2]
    cross_cols = sensors // scen_shards
    gram_cols = modes // scen_shards
    readings = observed.astype(jnp.float32).reshape(step_count, local_scen, scen_shards, cross_cols)
    readings = readings.transpose(2, 0, 1, 3)
    payload = jnp.concatenate(
        [jnp.broadcast_to(states[None], (scen_shards,) + states.shape), readings], axis=3
    )
    received = lax.all_to_all(payload, "scen", 0, 0, tiled=True)
    received = received.reshape(scen_shards, step_count, local_scen, modes + cross_cols)
    received = received.transpose(1, 0, 2, 3).reshape(
        step_count, scen_shards * local_scen, modes + cross_cols
    )
    every = received[:, :, :modes]
    readings = received[:, :, modes:]
    column = lax.axis_index("scen") * gram_cols
    right = jnp.concatenate(
        [lax.dynamic_slice_in_dim(every, column, gram_cols, axis=2), readings], axis=2
    )
    joined = jnp.einsum("tsr,tso->ro", every, right, precision=highest) * normalize
    mine = joined
    stride = time_shards
    for size in tm_groups:
        stride //= size
        groups = [
            [base + k * stride for k in range(size)]
            for base in range(time_shards)
            if (base // stride) % size == 0
        ]
        pieces = mine.reshape(size, mine.shape[0] // size, mine.shape[1])
        mine = lax.all_to_all(pieces, "tm", 0, 0, tiled=True, axis_index_groups=groups).sum(axis=0)
    return (states, mine[:, :gram_cols], mine[:, gram_cols:])


def solution(mesh):
    in_specs = (
        P("tm", None, None),
        P(),
        P("tm"),
        P("tm", "scen", None),
        P("scen", None),
        P("tm", "scen", None),
    )
    out_specs = (P("tm", "scen", None), P("tm", "scen"), P("tm", "scen"))
    count = dict(zip(mesh.axis_names, mesh.devices.shape))["tm"]
    tm_groups = (count // 8, 8) if count % 8 == 0 and count > 8 else (count,)

    def on_device(*args):
        return on_device_body(tm_groups, *args)

    return jax.shard_map(
        on_device, mesh=mesh, in_specs=in_specs, out_specs=out_specs, check_vma=False
    )
```
